128 devices in a mesh: row: 32 (over x, z, y_hi), col: 4 (over y_lo, core).
Axes of the slice: x: 4, y: 4 (y_hi: 2, y_lo: 2; y = y_hi * 2 + y_lo), z: 4, core: 2. Of those that a mesh axis runs over, the one named last changes fastest.
Arguments:
- tokens: bfloat16 [256, 8192], P('row', 'col'), may hold values from -6 to 6
- gate_weight: bfloat16 [8192, 14336], P(None, ('row', 'col')), may hold values from -0.0625 to 0.0625
- up_weight: bfloat16 [8192, 14336], P(None, ('row', 'col')), may hold values from -0.0625 to 0.0625
- down_weight: bfloat16 [14336, 8192], P(('row', 'col')), may hold values from -0.1875 to 0.1875
- out_grad: bfloat16 [256, 8192], P('row', 'col'), may hold values from -1.796875 to 1.796875
Outputs:
- output: float32 [256, 8192], P('row', 'col')
- input_grad: float32 [256, 8192], P('row', 'col')
- grad_gate: bfloat16 [8192, 14336], P('col', 'row')
- grad_up: bfloat16 [8192, 14336], P('col', 'row')
- grad_down: bfloat16 [14336, 8192], P('row', 'col')
The draws below stay inside these ranges and needn't reach their ends.
All inputs are finite; a program needn't handle non-finite values.
Results may differ from the reference program's by a relative error of at most 0.0049.
Values may be sent and summed in bfloat16 or wider, within the bound.
No kernel may reach another device: no remote copies, remote signals or barrier semaphores. Data moves between devices by JAX's collectives and lax.ppermute only.
A program may use at most 64 MiB of HBM per device.

```python
import jax
import jax.numpy as jnp

D = 8192
FF = 14336
TOKENS = 256


def raised(values, key, source, target, parts, factor):
    owner, partner = [(jnp.arange(values.shape[position]) // (values.shape[position] // parts)).reshape([-1 if axis == position else 1 for axis in range(values.ndim)]) for position in (source, target)]
    chosen = jax.random.permutation(key, parts)[partner]
    strong = (owner == chosen) | (owner == (partner + parts // 2) % parts)
    return jnp.where(strong, factor * values, values)


def shard_levels(own_key, shape, shards, low, high):
    factor_of, own = 1.0, jax.random.fold_in(own_key, 6)
    for dim, parts in shards:
        draws = jnp.exp(jax.random.uniform(jax.random.fold_in(own, dim), (parts,), jnp.float32, low / len(shards), high / len(shards)))
        factor_of = factor_of * jnp.repeat(draws, shape[dim] // parts).reshape([-1 if axis == dim else 1 for axis in range(len(shape))])
    return factor_of


def gaussian(key, shape, spread, bound, split=(), held_as=jnp.bfloat16):
    array = jax.random.normal(key, shape, jnp.float32) * spread
    if len(split) > 0:
        array = shard_levels(key, shape, split, -0.22, 0.18) * array
    return jnp.clip(array, min=-bound, max=bound).astype(held_as)


def noise_with(rng, shape, spread, bound, shards, heavy, dtype=jnp.bfloat16):
    values = spread * jax.random.normal(rng, shape, jnp.float32)
    if shards:
        values = values * shard_levels(rng, shape, shards, -0.22, 0.18)
    return jnp.clip(raised(values, jax.random.fold_in(rng, 3), *heavy), -bound, bound).astype(dtype)


def setup_inputs(seed: int = 0) -> dict:
    arg_keys = jax.random.split(jax.random.key(seed), 6)
    tokens = gaussian(arg_keys[0], (TOKENS, D), 1.0, 6.0, ((0, 32), (1, 4)))
    gate_weight = gaussian(arg_keys[1], (D, FF), D ** -0.5, 0.0625, ((1, 128),))
    up_weight = gaussian(arg_keys[2], (D, FF), D ** -0.5, 0.0625, ((1, 128),))
    down_weight = noise_with(arg_keys[3], (FF, D), FF ** -0.5, 0.1875, ((0, 128),), (0, 1, 128, 5.5))
    out_grad = gaussian(arg_keys[4], (TOKENS, D), 0.3, 1.796875, ((0, 32), (1, 4)))
    return {"tokens": tokens, "gate_weight": gate_weight, "up_weight": up_weight, "down_weight": down_weight, "out_grad": out_grad}


def reference(tokens, gate_weight, up_weight, down_weight, out_grad):
    gate = jnp.dot(tokens, gate_weight, preferred_element_type=jnp.float32)
    up = jnp.dot(tokens, up_weight, preferred_element_type=jnp.float32)
    sig = jax.nn.sigmoid(gate)
    hidden = (gate * sig * up).astype(jnp.bfloat16)
    output = jnp.dot(hidden, down_weight, preferred_element_type=jnp.float32)
    hidden_grad = jnp.dot(out_grad, down_weight.T, preferred_element_type=jnp.float32)
    gate_grad = (hidden_grad * up * sig * (1.0 + gate * (1.0 - sig))).astype(jnp.bfloat16)
    up_grad = (hidden_grad * gate * sig).astype(jnp.bfloat16)
    input_grad = (jnp.dot(gate_grad, gate_weight.T, preferred_element_type=jnp.float32)
                  + jnp.dot(up_grad, up_weight.T, preferred_element_type=jnp.float32))
    grad_gate = jnp.dot(tokens.T, gate_grad, preferred_element_type=jnp.float32).astype(jnp.bfloat16)
    grad_up = jnp.dot(tokens.T, up_grad, preferred_element_type=jnp.float32).astype(jnp.bfloat16)
    grad_down = jnp.dot(hidden.T, out_grad, preferred_element_type=jnp.float32).astype(jnp.bfloat16)
    return output, input_grad, grad_gate, grad_up, grad_down
```

```python
import jax
import jax.numpy as jnp
from jax import lax
from jax.sharding import PartitionSpec as P


def contract_last(left, right):
    return lax.dot_general(
        left, right, (((1,), (1,)), ((), ())), preferred_element_type=jnp.float32
    )


def contract_first(left, right):
    return lax.dot_general(
        left, right, (((0,), (0,)), ((), ())), preferred_element_type=jnp.float32
    )


def gather_rows(block, axis, n):
    spread = jnp.broadcast_to(block[None], (n,) + block.shape)
    got = lax.all_to_all(spread, axis, split_axis=0, concat_axis=0, tiled=True)
    return got.reshape((n * block.shape[0],) + block.shape[1:])


def reduce_rows(part, axis, n):
    pieces = part.reshape((n, part.shape[0] // n) + part.shape[1:])
    got = lax.all_to_all(pieces, axis, split_axis=0, concat_axis=0, tiled=True)
    return jnp.sum(got, axis=0)


def shards(tokens, gate_weight, up_weight, down_weight, out_grad):
    n_row = lax.axis_size("row")
    n_col = lax.axis_size("col")
    unit = gate_weight.shape[1]
    joined = jnp.concatenate([gate_weight, up_weight], axis=1)
    gu_block = lax.all_to_all(joined, "col", split_axis=0, concat_axis=1, tiled=True)
    feat = gu_block.shape[0]
    down_block = lax.all_to_all(down_weight, "col", split_axis=1, concat_axis=0, tiled=True)

    both = gather_rows(jnp.stack([tokens, out_grad], axis=1), "row", n_row)
    full_tokens = both[:, 0]
    grad_full = both[:, 1]

    gu_part = jnp.dot(full_tokens, gu_block, preferred_element_type=jnp.float32)
    gu_sum = reduce_rows(gu_part, "col", n_col).reshape(-1, n_col, 2, unit)
    gate_sum = gu_sum[:, :, 0].reshape(gu_sum.shape[0], n_col * unit)
    up_sum = gu_sum[:, :, 1].reshape(gu_sum.shape[0], n_col * unit)
    sig = jax.nn.sigmoid(gate_sum)
    hidden_share = (gate_sum * sig * up_sum).astype(jnp.bfloat16)
    hidden = gather_rows(hidden_share, "col", n_col)

    term = jnp.dot(hidden, down_block, preferred_element_type=jnp.float32)
    output = reduce_rows(term, "row", n_row)

    dh_part = contract_last(grad_full, down_block)
    hidden_grad = reduce_rows(dh_part, "col", n_col)
    grad_down = contract_first(hidden, grad_full).astype(jnp.bfloat16)

    gate_grad = (hidden_grad * up_sum * sig * (1.0 + gate_sum * (1.0 - sig))).astype(jnp.bfloat16)
    up_grad = (hidden_grad * gate_sum * sig).astype(jnp.bfloat16)
    grads = gather_rows(jnp.stack([gate_grad, up_grad], axis=1), "col", n_col)
    gate_all = grads[:, 0]
    up_all = grads[:, 1]

    gu4 = gu_block.reshape(feat, n_col, 2, unit)
    gate_block = gu4[:, :, 0].reshape(feat, n_col * unit)
    up_block = gu4[:, :, 1].reshape(feat, n_col * unit)
    in_part = contract_last(gate_all, gate_block) + contract_last(up_all, up_block)
    input_grad = reduce_rows(in_part, "row", n_row)
    grad_gate = contract_first(full_tokens, gate_all).astype(jnp.bfloat16)
    grad_up = contract_first(full_tokens, up_all).astype(jnp.bfloat16)
    return (output, input_grad, grad_gate, grad_up, grad_down)


def solution(mesh):
    placed = (
        P("row", "col"),
        P(None, ("row", "col")),
        P(None, ("row", "col")),
        P(("row", "col"), None),
        P("row", "col"),
    )
    return jax.shard_map(
        shards,
        mesh=mesh,
        in_specs=placed,
        out_specs=(
            P("row", "col"),
            P("row", "col"),
            P("col", "row"),
            P("col", "row"),
            P("row", "col"),
        ),
        check_vma=False,
    )
```

```python
import jax
import jax.numpy as jnp
from jax import lax
from jax.sharding import PartitionSpec as P


def contract_last(left, right):
    return lax.dot_general(
        left, right, (((1,), (1,)), ((), ())), preferred_element_type=jnp.float32
    )


def contract_first(left, right):
    return lax.dot_general(
        left, right, (((0,), (0,)), ((), ())), preferred_element_type=jnp.float32
    )


def gather_rows(block, axis, n):
    spread = jnp.broadcast_to(block[None], (n,) + block.shape)
    got = lax.all_to_all(spread, axis, split_axis=0, concat_axis=0, tiled=True)
    return got.reshape((n * block.shape[0],) + block.shape[1:])


def reduce_rows(part, axis, n):
    pieces = part.reshape((n, part.shape[0] // n) + part.shape[1:])
    got = lax.all_to_all(pieces, axis, split_axis=0, concat_axis=0, tiled=True)
    return jnp.sum(got, axis=0)


def swap(x, k, n):
    return lax.ppermute(x, "col", perm=[(i, i ^ k) for i in range(n)])


def piece(x, index, size, axis):
    return lax.dynamic_slice_in_dim(x, index * size, size, axis)


def col_scatter(x, axis, n):
    me = lax.axis_index("col")
    size = x.shape[axis] // n
    got = [piece(x, me, size, axis)]
    for k in range(1, n):
        got.append(swap(piece(x, me ^ k, size, axis), k, n))
    stacked = jnp.stack(got)
    order = jnp.arange(n, dtype=jnp.int32) ^ me
    return jnp.take(stacked, order, axis=0)


def col_gather(x, n):
    me = lax.axis_index("col")
    got = [x] + [swap(x, k, n) for k in range(1, n)]
    stacked = jnp.stack(got)
    order = jnp.arange(n, dtype=jnp.int32) ^ me
    return jnp.take(stacked, order, axis=0)


def col_reduce(x, n):
    me = lax.axis_index("col")
    size = x.shape[0] // n
    total = piece(x, me, size, 0)
    for k in range(1, n):
        total = total + swap(piece(x, me ^ k, size, 0), k, n)
    return total


def shards(tokens, gate_weight, up_weight, down_weight, out_grad):
    n_row = lax.axis_size("row")
    n_col = lax.axis_size("col")
    unit = gate_weight.shape[1]
    joined = jnp.concatenate([gate_weight, up_weight], axis=1)
    gu_stack = col_scatter(joined, 0, n_col)
    feat = gu_stack.shape[1]
    gu_block = gu_stack.reshape(n_col, feat, 2, unit)
    gate_block = gu_block[:, :, 0].transpose(1, 0, 2).reshape(feat, n_col * unit)
    up_block = gu_block[:, :, 1].transpose(1, 0, 2).reshape(feat, n_col * unit)
    down_block = col_scatter(down_weight, 1, n_col).reshape(n_col * unit, feat)

    both = gather_rows(jnp.stack([tokens, out_grad], axis=1), "row", n_row)
    full_tokens = both[:, 0]
    grad_full = both[:, 1]

    gu_w = jnp.concatenate([gate_block, up_block], axis=1)
    gu_part = jnp.dot(full_tokens, gu_w, preferred_element_type=jnp.float32)
    gu_sum = col_reduce(gu_part, n_col)
    gate_sum = gu_sum[:, : n_col * unit]
    up_sum = gu_sum[:, n_col * unit :]
    sig = jax.nn.sigmoid(gate_sum)
    hidden_share = (gate_sum * sig * up_sum).astype(jnp.bfloat16)
    hidden = col_gather(hidden_share, n_col).reshape(-1, n_col * unit)

    term = jnp.dot(hidden, down_block, preferred_element_type=jnp.float32)
    output = reduce_rows(term, "row", n_row)

    dh_part = contract_last(grad_full, down_block)
    hidden_grad = col_reduce(dh_part, n_col)
    grad_down = contract_first(hidden, grad_full).astype(jnp.bfloat16)

    gate_grad = (hidden_grad * up_sum * sig * (1.0 + gate_sum * (1.0 - sig))).astype(jnp.bfloat16)
    up_grad = (hidden_grad * gate_sum * sig).astype(jnp.bfloat16)
    grads = col_gather(jnp.concatenate([gate_grad, up_grad], axis=1), n_col)
    grads = grads.reshape(-1, 2 * n_col * unit)

    in_part = contract_last(grads, gu_w)
    input_grad = reduce_rows(in_part, "row", n_row)
    grad_gu = contract_first(full_tokens, grads)
    grad_gate = grad_gu[:, : n_col * unit].astype(jnp.bfloat16)
    grad_up = grad_gu[:, n_col * unit :].astype(jnp.bfloat16)
    return (output, input_grad, grad_gate, grad_up, grad_down)


def solution(mesh):
    placed = (
        P("row", "col"),
        P(None, ("row", "col")),
        P(None, ("row", "col")),
        P(("row", "col"), None),
        P("row", "col"),
    )
    return jax.shard_map(
        shards,
        mesh=mesh,
        in_specs=placed,
        out_specs=(
            P("row", "col"),
            P("row", "col"),
            P("col", "row"),
            P("col", "row"),
            P("row", "col"),
        ),
        check_vma=False,
    )
```

```python
import jax
import jax.numpy as jnp
from jax import lax
from jax.sharding import PartitionSpec as P


def contract_last(left, right):
    return lax.dot_general(
        left, right, (((1,), (1,)), ((), ())), preferred_element_type=jnp.float32
    )


def contract_first(left, right):
    return lax.dot_general(
        left, right, (((0,), (0,)), ((), ())), preferred_element_type=jnp.float32
    )


def gather_rows(block, axis, n):
    spread = jnp.broadcast_to(block[None], (n,) + block.shape)
    got = lax.all_to_all(spread, axis, split_axis=0, concat_axis=0, tiled=True)
    return got.reshape((n * block.shape[0],) + block.shape[1:])


def reduce_rows(part, axis, n):
    pieces = part.reshape((n, part.shape[0] // n) + part.shape[1:])
    got = lax.all_to_all(pieces, axis, split_axis=0, concat_axis=0, tiled=True)
    return jnp.sum(got, axis=0)


def swap(x, k, n):
    return lax.ppermute(x, "col", perm=[(i, i ^ k) for i in range(n)])


def piece(x, index, size, axis):
    return lax.dynamic_slice_in_dim(x, index * size, size, axis)


def place(pieces, me, axis):
    shape = list(pieces[0].shape)
    shape.insert(axis, len(pieces))
    out = jnp.zeros(shape, pieces[0].dtype)
    for k, p in enumerate(pieces):
        start = [0] * len(shape)
        start[axis] = me ^ k
        out = lax.dynamic_update_slice(out, jnp.expand_dims(p, axis), start)
    return out


def col_scatter(x, axis, n):
    me = lax.axis_index("col")
    size = x.shape[axis] // n
    got = [piece(x, me, size, axis)]
    for k in range(1, n):
        got.append(swap(piece(x, me ^ k, size, axis), k, n))
    return got


def col_gather(x, n):
    me = lax.axis_index("col")
    got = [x] + [swap(x, k, n) for k in range(1, n)]
    return place(got, me, 0)


def col_reduce(x, n):
    me = lax.axis_index("col")
    size = x.shape[0] // n
    total = piece(x, me, size, 0)
    for k in range(1, n):
        total = total + swap(piece(x, me ^ k, size, 0), k, n)
    return total


def shards(tokens, gate_weight, up_weight, down_weight, out_grad):
    n_row = lax.axis_size("row")
    n_col = lax.axis_size("col")
    me = lax.axis_index("col")
    unit = gate_weight.shape[1]
    joined = jnp.concatenate([gate_weight, up_weight], axis=1)
    gu_rel = col_scatter(joined, 0, n_col)
    down_rel = col_scatter(down_weight, 1, n_col)

    both = gather_rows(jnp.stack([tokens, out_grad], axis=1), "row", n_row)
    full_tokens = both[:, 0]
    grad_full = both[:, 1]
    count = full_tokens.shape[0]

    gu_part = place([jnp.dot(full_tokens, w, preferred_element_type=jnp.float32) for w in gu_rel], me, 1)
    gu_sum = col_reduce(gu_part, n_col)
    share = gu_sum.shape[0]
    gate_sum = gu_sum[:, :, :unit].reshape(share, n_col * unit)
    up_sum = gu_sum[:, :, unit:].reshape(share, n_col * unit)
    sig = jax.nn.sigmoid(gate_sum)
    hidden_share = (gate_sum * sig * up_sum).astype(jnp.bfloat16)
    hidden = col_gather(hidden_share, n_col).reshape(count, n_col * unit)

    term = None
    for k, w in enumerate(down_rel):
        h = lax.dynamic_slice_in_dim(hidden, (me ^ k) * unit, unit, 1)
        t = jnp.dot(h, w, preferred_element_type=jnp.float32)
        term = t if term is None else term + t
    output = reduce_rows(term, "row", n_row)

    dh_part = place([contract_last(grad_full, w) for w in down_rel], me, 1)
    hidden_grad = col_reduce(dh_part, n_col).reshape(share, n_col * unit)
    grad_down = contract_first(hidden, grad_full).astype(jnp.bfloat16)

    gate_grad = (hidden_grad * up_sum * sig * (1.0 + gate_sum * (1.0 - sig))).astype(jnp.bfloat16)
    up_grad = (hidden_grad * gate_sum * sig).astype(jnp.bfloat16)
    joined_grad = jnp.concatenate(
        [gate_grad.reshape(share, n_col, unit), up_grad.reshape(share, n_col, unit)], axis=2
    )
    grads = col_gather(joined_grad, n_col).reshape(count, n_col, 2 * unit)

    in_part = None
    for k, w in enumerate(gu_rel):
        g = lax.dynamic_index_in_dim(grads, me ^ k, 1, keepdims=False)
        t = contract_last(g, w)
        in_part = t if in_part is None else in_part + t
    input_grad = reduce_rows(in_part, "row", n_row)
    grad_gu = contract_first(full_tokens, grads.reshape(count, n_col * 2 * unit))
    grad_gu = grad_gu.reshape(-1, n_col, 2 * unit)
    grad_gate = grad_gu[:, :, :unit].reshape(-1, n_col * unit).astype(jnp.bfloat16)
    grad_up = grad_gu[:, :, unit:].reshape(-1, n_col * unit).astype(jnp.bfloat16)
    return (output, input_grad, grad_gate, grad_up, grad_down)


def solution(mesh):
    placed = (
        P("row", "col"),
        P(None, ("row", "col")),
        P(None, ("row", "col")),
        P(("row", "col"), None),
        P("row", "col"),
    )
    return jax.shard_map(
        shards,
        mesh=mesh,
        in_specs=placed,
        out_specs=(
            P("row", "col"),
            P("row", "col"),
            P("col", "row"),
            P("col", "row"),
            P("row", "col"),
        ),
        check_vma=False,
    )
```

```python
import jax
import jax.numpy as jnp
from jax import lax
from jax.sharding import PartitionSpec as P


def contract_last(left, right):
    return lax.dot_general(
        left, right, (((1,), (1,)), ((), ())), preferred_element_type=jnp.float32
    )


def contract_first(left, right):
    return lax.dot_general(
        left, right, (((0,), (0,)), ((), ())), preferred_element_type=jnp.float32
    )


def gather_rows(block, axis, n):
    spread = jnp.broadcast_to(block[None], (n,) + block.shape)
    got = lax.all_to_all(spread, axis, split_axis=0, concat_axis=0, tiled=True)
    return got.reshape((n * block.shape[0],) + block.shape[1:])


def reduce_rows(part, axis, n):
    pieces = part.reshape((n, part.shape[0] // n) + part.shape[1:])
    got = lax.all_to_all(pieces, axis, split_axis=0, concat_axis=0, tiled=True)
    return jnp.sum(got, axis=0)


def swap(x, k, n):
    return lax.ppermute(x, "col", perm=[(i, i ^ k) for i in range(n)])


def piece(x, index, size, axis):
    return lax.dynamic_slice_in_dim(x, index * size, size, axis)


def place(pieces, me, axis):
    shape = list(pieces[0].shape)
    shape.insert(axis, len(pieces))
    out = jnp.zeros(shape, pieces[0].dtype)
    for k, p in enumerate(pieces):
        start = [0] * len(shape)
        start[axis] = me ^ k
        out = lax.dynamic_update_slice(out, jnp.expand_dims(p, axis), start)
    return out


def col_scatter(x, axis, n):
    me = lax.axis_index("col")
    size = x.shape[axis] // n
    got = [piece(x, me, size, axis)]
    for k in range(1, n):
        got.append(swap(piece(x, me ^ k, size, axis), k, n))
    return got


def col_gather(x, n):
    me = lax.axis_index("col")
    got = [x] + [swap(x, k, n) for k in range(1, n)]
    return place(got, me, 0)


def col_reduce(x, n):
    me = lax.axis_index("col")
    size = x.shape[0] // n
    total = piece(x, me, size, 0)
    for k in range(1, n):
        total = total + swap(piece(x, me ^ k, size, 0), k, n)
    return total


def shards(tokens, gate_weight, up_weight, down_weight, out_grad):
    n_row = lax.axis_size("row")
    n_col = lax.axis_size("col")
    me = lax.axis_index("col")
    unit = gate_weight.shape[1]
    joined = jnp.concatenate([gate_weight, up_weight], axis=1)
    feat = joined.shape[0] // n_col
    gu_out = [piece(joined, me ^ k, feat, 0) for k in range(n_col)]
    down_out = [piece(down_weight, me ^ k, feat, 1) for k in range(n_col)]
    pair = jnp.stack([tokens, out_grad], axis=1)
    gu_out, down_out, pair = lax.optimization_barrier((gu_out, down_out, pair))
    gu_rel = [gu_out[0]] + [swap(gu_out[k], k, n_col) for k in range(1, n_col)]
    down_rel = [down_out[0]] + [swap(down_out[k], k, n_col) for k in range(1, n_col)]

    both = gather_rows(pair, "row", n_row)
    full_tokens = both[:, 0]
    grad_full = both[:, 1]
    count = full_tokens.shape[0]

    gu_part = place([jnp.dot(full_tokens, w, preferred_element_type=jnp.float32) for w in gu_rel], me, 1)
    gu_sum = col_reduce(gu_part, n_col)
    share = gu_sum.shape[0]
    gate_sum = gu_sum[:, :, :unit].reshape(share, n_col * unit)
    up_sum = gu_sum[:, :, unit:].reshape(share, n_col * unit)
    sig = jax.nn.sigmoid(gate_sum)
    hidden_share = (gate_sum * sig * up_sum).astype(jnp.bfloat16)
    hidden = col_gather(hidden_share, n_col).reshape(count, n_col * unit)

    term = None
    for k, w in enumerate(down_rel):
        h = lax.dynamic_slice_in_dim(hidden, (me ^ k) * unit, unit, 1)
        t = jnp.dot(h, w, preferred_element_type=jnp.float32)
        term = t if term is None else term + t
    output = reduce_rows(term, "row", n_row)

    dh_part = place([contract_last(grad_full, w) for w in down_rel], me, 1)
    hidden_grad = col_reduce(dh_part, n_col).reshape(share, n_col * unit)
    grad_down = contract_first(hidden, grad_full).astype(jnp.bfloat16)

    gate_grad = (hidden_grad * up_sum * sig * (1.0 + gate_sum * (1.0 - sig))).astype(jnp.bfloat16)
    up_grad = (hidden_grad * gate_sum * sig).astype(jnp.bfloat16)
    joined_grad = jnp.concatenate(
        [gate_grad.reshape(share, n_col, unit), up_grad.reshape(share, n_col, unit)], axis=2
    )
    grads = col_gather(joined_grad, n_col).reshape(count, n_col, 2 * unit)

    in_part = None
    for k, w in enumerate(gu_rel):
        g = lax.dynamic_index_in_dim(grads, me ^ k, 1, keepdims=False)
        t = contract_last(g, w)
        in_part = t if in_part is None else in_part + t
    input_grad = reduce_rows(in_part, "row", n_row)
    grad_gu = contract_first(full_tokens, grads.reshape(count, n_col * 2 * unit))
    grad_gu = grad_gu.reshape(-1, n_col, 2 * unit)
    grad_gate = grad_gu[:, :, :unit].reshape(-1, n_col * unit).astype(jnp.bfloat16)
    grad_up = grad_gu[:, :, unit:].reshape(-1, n_col * unit).astype(jnp.bfloat16)
    return (output, input_grad, grad_gate, grad_up, grad_down)


def solution(mesh):
    placed = (
        P("row", "col"),
        P(None, ("row", "col")),
        P(None, ("row", "col")),
        P(("row", "col"), None),
        P("row", "col"),
    )
    return jax.shard_map(
        shards,
        mesh=mesh,
        in_specs=placed,
        out_specs=(
            P("row", "col"),
            P("row", "col"),
            P("col", "row"),
            P("col", "row"),
            P("row", "col"),
        ),
        check_vma=False,
    )
```

```python
import jax
import jax.numpy as jnp
from jax import lax
from jax.sharding import PartitionSpec as P


def contract_last(left, right):
    return lax.dot_general(
        left, right, (((1,), (1,)), ((), ())), preferred_element_type=jnp.float32
    )


def contract_first(left, right):
    return lax.dot_general(
        left, right, (((0,), (0,)), ((), ())), preferred_element_type=jnp.float32
    )


def gather_rows(block, axis, n):
    spread = jnp.broadcast_to(block[None], (n,) + block.shape)
    got = lax.all_to_all(spread, axis, split_axis=0, concat_axis=0, tiled=True)
    return got.reshape((n * block.shape[0],) + block.shape[1:])


def reduce_rows(part, axis, n):
    pieces = part.reshape((n, part.shape[0] // n) + part.shape[1:]).astype(jnp.bfloat16)
    got = lax.all_to_all(pieces, axis, split_axis=0, concat_axis=0, tiled=True)
    return jnp.sum(got.astype(jnp.float32), axis=0)


def swap(x, k, n):
    return lax.ppermute(x, "col", perm=[(i, i ^ k) for i in range(n)])


def piece(x, index, size, axis):
    return lax.dynamic_slice_in_dim(x, index * size, size, axis)


def place(pieces, me, axis):
    shape = list(pieces[0].shape)
    shape.insert(axis, len(pieces))
    out = jnp.zeros(shape, pieces[0].dtype)
    for k, p in enumerate(pieces):
        start = [0] * len(shape)
        start[axis] = me ^ k
        out = lax.dynamic_update_slice(out, jnp.expand_dims(p, axis), start)
    return out


def col_scatter(x, axis, n):
    me = lax.axis_index("col")
    size = x.shape[axis] // n
    got = [piece(x, me, size, axis)]
    for k in range(1, n):
        got.append(swap(piece(x, me ^ k, size, axis), k, n))
    return got


def col_gather(x, n):
    me = lax.axis_index("col")
    got = [x] + [swap(x, k, n) for k in range(1, n)]
    return place(got, me, 0)


def col_reduce(x, n):
    me = lax.axis_index("col")
    size = x.shape[0] // n
    total = piece(x, me, size, 0)
    for k in range(1, n):
        total = total + swap(piece(x, me ^ k, size, 0), k, n)
    return total


def shards(tokens, gate_weight, up_weight, down_weight, out_grad):
    n_row = lax.axis_size("row")
    n_col = lax.axis_size("col")
    me = lax.axis_index("col")
    unit = gate_weight.shape[1]
    joined = jnp.concatenate([gate_weight, up_weight], axis=1)
    gu_rel = col_scatter(joined, 0, n_col)
    down_rel = col_scatter(down_weight, 1, n_col)

    both = gather_rows(jnp.stack([tokens, out_grad], axis=1), "row", n_row)
    full_tokens = both[:, 0]
    grad_full = both[:, 1]
    count = full_tokens.shape[0]

    gu_part = place([jnp.dot(full_tokens, w, preferred_element_type=jnp.float32) for w in gu_rel], me, 1)
    gu_sum = col_reduce(gu_part, n_col)
    share = gu_sum.shape[0]
    gate_sum = gu_sum[:, :, :unit].reshape(share, n_col * unit)
    up_sum = gu_sum[:, :, unit:].reshape(share, n_col * unit)
    sig = jax.nn.sigmoid(gate_sum)
    hidden_share = (gate_sum * sig * up_sum).astype(jnp.bfloat16)
    hidden = col_gather(hidden_share, n_col).reshape(count, n_col * unit)

    term = None
    for k, w in enumerate(down_rel):
        h = lax.dynamic_slice_in_dim(hidden, (me ^ k) * unit, unit, 1)
        t = jnp.dot(h, w, preferred_element_type=jnp.float32)
        term = t if term is None else term + t
    output = reduce_rows(term, "row", n_row)

    dh_part = place([contract_last(grad_full, w) for w in down_rel], me, 1)
    hidden_grad = col_reduce(dh_part, n_col).reshape(share, n_col * unit)
    grad_down = contract_first(hidden, grad_full).astype(jnp.bfloat16)

    gate_grad = (hidden_grad * up_sum * sig * (1.0 + gate_sum * (1.0 - sig))).astype(jnp.bfloat16)
    up_grad = (hidden_grad * gate_sum * sig).astype(jnp.bfloat16)
    joined_grad = jnp.concatenate(
        [gate_grad.reshape(share, n_col, unit), up_grad.reshape(share, n_col, unit)], axis=2
    )
    grads = col_gather(joined_grad, n_col).reshape(count, n_col, 2 * unit)

    in_part = None
    for k, w in enumerate(gu_rel):
        g = lax.dynamic_index_in_dim(grads, me ^ k, 1, keepdims=False)
        t = contract_last(g, w)
        in_part = t if in_part is None else in_part + t
    input_grad = reduce_rows(in_part, "row", n_row)
    grad_gu = contract_first(full_tokens, grads.reshape(count, n_col * 2 * unit))
    grad_gu = grad_gu.reshape(-1, n_col, 2 * unit)
    grad_gate = grad_gu[:, :, :unit].reshape(-1, n_col * unit).astype(jnp.bfloat16)
    grad_up = grad_gu[:, :, unit:].reshape(-1, n_col * unit).astype(jnp.bfloat16)
    return (output, input_grad, grad_gate, grad_up, grad_down)


def solution(mesh):
    placed = (
        P("row", "col"),
        P(None, ("row", "col")),
        P(None, ("row", "col")),
        P(("row", "col"), None),
        P("row", "col"),
    )
    return jax.shard_map(
        shards,
        mesh=mesh,
        in_specs=placed,
        out_specs=(
            P("row", "col"),
            P("row", "col"),
            P("col", "row"),
            P("col", "row"),
            P("row", "col"),
        ),
        check_vma=False,
    )
```

```python
import jax
import jax.numpy as jnp
from jax import lax
from jax.sharding import PartitionSpec as P


def contract_last(left, right):
    return lax.dot_general(
        left, right, (((1,), (1,)), ((), ())), preferred_element_type=jnp.float32
    )


def contract_first(left, right):
    return lax.dot_general(
        left, right, (((0,), (0,)), ((), ())), preferred_element_type=jnp.float32
    )


def gather_rows(block, axis, n):
    spread = jnp.broadcast_to(block[None], (n,) + block.shape)
    got = lax.all_to_all(spread, axis, split_axis=0, concat_axis=0, tiled=True)
    return got.reshape((n * block.shape[0],) + block.shape[1:])


def reduce_rows(part, axis, n):
    pieces = part.reshape((n, part.shape[0] // n) + part.shape[1:]).astype(jnp.bfloat16)
    got = lax.all_to_all(pieces, axis, split_axis=0, concat_axis=0, tiled=True)
    return jnp.sum(got.astype(jnp.float32), axis=0)


def swap(x, k, n):
    return lax.ppermute(x, "col", perm=[(i, i ^ k) for i in range(n)])


def piece(x, index, size, axis):
    return lax.dynamic_slice_in_dim(x, index * size, size, axis)


def place(pieces, me, axis):
    shape = list(pieces[0].shape)
    shape.insert(axis, len(pieces))
    out = jnp.zeros(shape, pieces[0].dtype)
    for k, p in enumerate(pieces):
        start = [0] * len(shape)
        start[axis] = me ^ k
        out = lax.dynamic_update_slice(out, jnp.expand_dims(p, axis), start)
    return out


def col_scatter(x, axis, n):
    me = lax.axis_index("col")
    size = x.shape[axis] // n
    got = [piece(x, me, size, axis)]
    for k in range(1, n):
        got.append(swap(piece(x, me ^ k, size, axis), k, n))
    return got


def col_gather(x, n):
    me = lax.axis_index("col")
    got = [x] + [swap(x, k, n) for k in range(1, n)]
    return place(got, me, 0)


def col_reduce(x, n):
    me = lax.axis_index("col")
    size = x.shape[0] // n
    total = piece(x, me, size, 0)
    for k in range(1, n):
        total = total + swap(piece(x, me ^ k, size, 0), k, n)
    return total


def shards(tokens, gate_weight, up_weight, down_weight, out_grad):
    n_row = lax.axis_size("row")
    n_col = lax.axis_size("col")
    me = lax.axis_index("col")
    unit = gate_weight.shape[1]
    joined = jnp.concatenate([gate_weight, up_weight], axis=1)
    gu_rel = col_scatter(joined, 0, n_col)
    down_rel = col_scatter(down_weight, 1, n_col)

    both = gather_rows(jnp.stack([tokens, out_grad], axis=1), "row", n_row)
    full_tokens = both[:, 0]
    grad_full = both[:, 1]
    count = full_tokens.shape[0]

    gu_part = place([jnp.dot(full_tokens, w, preferred_element_type=jnp.float32) for w in gu_rel], me, 1)
    gu_sum = col_reduce(gu_part, n_col)
    share = gu_sum.shape[0]
    gate_sum = gu_sum[:, :, :unit].reshape(share, n_col * unit)
    up_sum = gu_sum[:, :, unit:].reshape(share, n_col * unit)
    sig = jax.nn.sigmoid(gate_sum)
    hidden_share = (gate_sum * sig * up_sum).astype(jnp.bfloat16)
    hidden = col_gather(hidden_share, n_col).reshape(count, n_col * unit)

    term = None
    for k, w in enumerate(down_rel):
        h = lax.dynamic_slice_in_dim(hidden, (me ^ k) * unit, unit, 1)
        t = jnp.dot(h, w, preferred_element_type=jnp.float32)
        term = t if term is None else term + t

    dh_part = place([contract_last(grad_full, w) for w in down_rel], me, 1)
    hidden_grad = col_reduce(dh_part, n_col).reshape(share, n_col * unit)
    grad_down = contract_first(hidden, grad_full).astype(jnp.bfloat16)

    gate_grad = (hidden_grad * up_sum * sig * (1.0 + gate_sum * (1.0 - sig))).astype(jnp.bfloat16)
    up_grad = (hidden_grad * gate_sum * sig).astype(jnp.bfloat16)
    joined_grad = jnp.concatenate(
        [gate_grad.reshape(share, n_col, unit), up_grad.reshape(share, n_col, unit)], axis=2
    )
    grads = col_gather(joined_grad, n_col).reshape(count, n_col, 2 * unit)

    in_part = None
    for k, w in enumerate(gu_rel):
        g = lax.dynamic_index_in_dim(grads, me ^ k, 1, keepdims=False)
        t = contract_last(g, w)
        in_part = t if in_part is None else in_part + t
    summed = reduce_rows(jnp.stack([term, in_part], axis=1), "row", n_row)
    output = summed[:, 0]
    input_grad = summed[:, 1]
    grad_gu = contract_first(full_tokens, grads.reshape(count, n_col * 2 * unit))
    grad_gu = grad_gu.reshape(-1, n_col, 2 * unit)
    grad_gate = grad_gu[:, :, :unit].reshape(-1, n_col * unit).astype(jnp.bfloat16)
    grad_up = grad_gu[:, :, unit:].reshape(-1, n_col * unit).astype(jnp.bfloat16)
    return (output, input_grad, grad_gate, grad_up, grad_down)


def solution(mesh):
    placed = (
        P("row", "col"),
        P(None, ("row", "col")),
        P(None, ("row", "col")),
        P(("row", "col"), None),
        P("row", "col"),
    )
    return jax.shard_map(
        shards,
        mesh=mesh,
        in_specs=placed,
        out_specs=(
            P("row", "col"),
            P("row", "col"),
            P("col", "row"),
            P("col", "row"),
            P("row", "col"),
        ),
        check_vma=False,
    )
```

```python
import jax
import jax.numpy as jnp
from jax import lax
from jax.sharding import PartitionSpec as P


def contract_last(left, right):
    return lax.dot_general(
        left, right, (((1,), (1,)), ((), ())), preferred_element_type=jnp.float32
    )


def contract_first(left, right):
    return lax.dot_general(
        left, right, (((0,), (0,)), ((), ())), preferred_element_type=jnp.float32
    )


def gather_rows(block, axis, n):
    spread = jnp.broadcast_to(block[None], (n,) + block.shape)
    got = lax.all_to_all(spread, axis, split_axis=0, concat_axis=0, tiled=True)
    return got.reshape((n * block.shape[0],) + block.shape[1:])


def reduce_rows(part, axis, n):
    pieces = part.reshape((n, part.shape[0] // n) + part.shape[1:]).astype(jnp.bfloat16)
    got = lax.all_to_all(pieces, axis, split_axis=0, concat_axis=0, tiled=True)
    return jnp.sum(got.astype(jnp.float32), axis=0)


def row_tree(part, axis):
    me = lax.axis_index(axis)
    n = lax.axis_size(axis)
    y, z, x = me % 2, (me // 2) % 4, me // 8
    rows = part.shape[0] // n
    view = part.reshape((4, 4, 2, rows) + part.shape[1:])

    def swap_row(v, mask):
        return lax.ppermute(v.astype(jnp.bfloat16), axis, perm=[(i, i ^ mask) for i in range(n)])

    acc = lax.dynamic_index_in_dim(view, y, 2, keepdims=False)
    acc = acc + swap_row(lax.dynamic_index_in_dim(view, y ^ 1, 2, keepdims=False), 1).astype(jnp.float32)
    total = lax.dynamic_index_in_dim(acc, z, 1, keepdims=False)
    for k in range(1, 4):
        sent = lax.dynamic_index_in_dim(acc, z ^ k, 1, keepdims=False)
        total = total + swap_row(sent, k << 1).astype(jnp.float32)
    out = lax.dynamic_index_in_dim(total, x, 0, keepdims=False)
    for k in range(1, 4):
        sent = lax.dynamic_index_in_dim(total, x ^ k, 0, keepdims=False)
        out = out + swap_row(sent, k << 3).astype(jnp.float32)
    return out


def swap(x, k, n):
    return lax.ppermute(x, "col", perm=[(i, i ^ k) for i in range(n)])


def piece(x, index, size, axis):
    return lax.dynamic_slice_in_dim(x, index * size, size, axis)


def place(pieces, me, axis):
    shape = list(pieces[0].shape)
    shape.insert(axis, len(pieces))
    out = jnp.zeros(shape, pieces[0].dtype)
    for k, p in enumerate(pieces):
        start = [0] * len(shape)
        start[axis] = me ^ k
        out = lax.dynamic_update_slice(out, jnp.expand_dims(p, axis), start)
    return out


def col_scatter(x, axis, n):
    me = lax.axis_index("col")
    size = x.shape[axis] // n
    got = [piece(x, me, size, axis)]
    for k in range(1, n):
        got.append(swap(piece(x, me ^ k, size, axis), k, n))
    return got


def col_gather(x, n):
    me = lax.axis_index("col")
    got = [x] + [swap(x, k, n) for k in range(1, n)]
    return place(got, me, 0)


def col_reduce(x, n):
    me = lax.axis_index("col")
    size = x.shape[0] // n
    total = piece(x, me, size, 0)
    for k in range(1, n):
        total = total + swap(piece(x, me ^ k, size, 0), k, n)
    return total


def shards(tokens, gate_weight, up_weight, down_weight, out_grad):
    n_row = lax.axis_size("row")
    n_col = lax.axis_size("col")
    me = lax.axis_index("col")
    unit = gate_weight.shape[1]
    joined = jnp.concatenate([gate_weight, up_weight], axis=1)
    gu_rel = col_scatter(joined, 0, n_col)
    down_rel = col_scatter(down_weight, 1, n_col)

    both = gather_rows(jnp.stack([tokens, out_grad], axis=1), "row", n_row)
    full_tokens = both[:, 0]
    grad_full = both[:, 1]
    count = full_tokens.shape[0]

    gu_part = place([jnp.dot(full_tokens, w, preferred_element_type=jnp.float32) for w in gu_rel], me, 1)
    gu_sum = col_reduce(gu_part, n_col)
    share = gu_sum.shape[0]
    gate_sum = gu_sum[:, :, :unit].reshape(share, n_col * unit)
    up_sum = gu_sum[:, :, unit:].reshape(share, n_col * unit)
    sig = jax.nn.sigmoid(gate_sum)
    hidden_share = (gate_sum * sig * up_sum).astype(jnp.bfloat16)
    hidden = col_gather(hidden_share, n_col).reshape(count, n_col * unit)

    term = None
    for k, w in enumerate(down_rel):
        h = lax.dynamic_slice_in_dim(hidden, (me ^ k) * unit, unit, 1)
        t = jnp.dot(h, w, preferred_element_type=jnp.float32)
        term = t if term is None else term + t
    output = row_tree(term, "row")

    dh_part = place([contract_last(grad_full, w) for w in down_rel], me, 1)
    hidden_grad = col_reduce(dh_part, n_col).reshape(share, n_col * unit)
    grad_down = contract_first(hidden, grad_full).astype(jnp.bfloat16)

    gate_grad = (hidden_grad * up_sum * sig * (1.0 + gate_sum * (1.0 - sig))).astype(jnp.bfloat16)
    up_grad = (hidden_grad * gate_sum * sig).astype(jnp.bfloat16)
    joined_grad = jnp.concatenate(
        [gate_grad.reshape(share, n_col, unit), up_grad.reshape(share, n_col, unit)], axis=2
    )
    grads = col_gather(joined_grad, n_col).reshape(count, n_col, 2 * unit)

    in_part = None
    for k, w in enumerate(gu_rel):
        g = lax.dynamic_index_in_dim(grads, me ^ k, 1, keepdims=False)
        t = contract_last(g, w)
        in_part = t if in_part is None else in_part + t
    input_grad = reduce_rows(in_part, "row", n_row)
    grad_gu = contract_first(full_tokens, grads.reshape(count, n_col * 2 * unit))
    grad_gu = grad_gu.reshape(-1, n_col, 2 * unit)
    grad_gate = grad_gu[:, :, :unit].reshape(-1, n_col * unit).astype(jnp.bfloat16)
    grad_up = grad_gu[:, :, unit:].reshape(-1, n_col * unit).astype(jnp.bfloat16)
    return (output, input_grad, grad_gate, grad_up, grad_down)


def solution(mesh):
    placed = (
        P("row", "col"),
        P(None, ("row", "col")),
        P(None, ("row", "col")),
        P(("row", "col"), None),
        P("row", "col"),
    )
    return jax.shard_map(
        shards,
        mesh=mesh,
        in_specs=placed,
        out_specs=(
            P("row", "col"),
            P("row", "col"),
            P("col", "row"),
            P("col", "row"),
            P("row", "col"),
        ),
        check_vma=False,
    )
```

```python
import jax
import jax.numpy as jnp
from jax import lax
from jax.sharding import PartitionSpec as P


def contract_last(left, right):
    return lax.dot_general(
        left, right, (((1,), (1,)), ((), ())), preferred_element_type=jnp.float32
    )


def contract_first(left, right):
    return lax.dot_general(
        left, right, (((0,), (0,)), ((), ())), preferred_element_type=jnp.float32
    )


def gather_rows(block, axis, n):
    spread = jnp.broadcast_to(block[None], (n,) + block.shape)
    got = lax.all_to_all(spread, axis, split_axis=0, concat_axis=0, tiled=True)
    return got.reshape((n * block.shape[0],) + block.shape[1:])


def reduce_rows(part, axis, n):
    pieces = part.reshape((n, part.shape[0] // n) + part.shape[1:]).astype(jnp.bfloat16)
    got = lax.all_to_all(pieces, axis, split_axis=0, concat_axis=0, tiled=True)
    return jnp.sum(got.astype(jnp.float32), axis=0)


def swap(x, k, n):
    return lax.ppermute(x, "col", perm=[(i, i ^ k) for i in range(n)])


def piece(x, index, size, axis):
    return lax.dynamic_slice_in_dim(x, index * size, size, axis)


def place(pieces, me, axis):
    shape = list(pieces[0].shape)
    shape.insert(axis, len(pieces))
    out = jnp.zeros(shape, pieces[0].dtype)
    for k, p in enumerate(pieces):
        start = [0] * len(shape)
        start[axis] = me ^ k
        out = lax.dynamic_update_slice(out, jnp.expand_dims(p, axis), start)
    return out


def col_scatter(x, axis, n):
    me = lax.axis_index("col")
    size = x.shape[axis] // n
    got = [piece(x, me, size, axis)]
    for k in range(1, n):
        got.append(swap(piece(x, me ^ k, size, axis), k, n))
    return got


def col_gather(x, n):
    me = lax.axis_index("col")
    got = [x] + [swap(x, k, n) for k in range(1, n)]
    return place(got, me, 0)


def col_reduce(x, n):
    me = lax.axis_index("col")
    size = x.shape[0] // n
    total = piece(x, me, size, 0)
    for k in range(1, n):
        total = total + swap(piece(x, me ^ k, size, 0), k, n)
    return total


def shards(tokens, gate_weight, up_weight, down_weight, out_grad):
    n_row = lax.axis_size("row")
    n_col = lax.axis_size("col")
    me = lax.axis_index("col")
    unit = gate_weight.shape[1]
    joined = jnp.concatenate([gate_weight, up_weight], axis=1)
    gu_rel = col_scatter(joined, 0, n_col)
    down_rel = col_scatter(down_weight, 1, n_col)

    pair = jnp.stack([tokens, out_grad], axis=1)
    pair, gu_near, down_near = lax.optimization_barrier((pair, gu_rel[1], down_rel[1]))
    gu_rel[1] = gu_near
    down_rel[1] = down_near
    both = gather_rows(pair, "row", n_row)
    full_tokens = both[:, 0]
    grad_full = both[:, 1]
    count = full_tokens.shape[0]

    gu_part = place([jnp.dot(full_tokens, w, preferred_element_type=jnp.float32) for w in gu_rel], me, 1)
    gu_sum = col_reduce(gu_part, n_col)
    share = gu_sum.shape[0]
    gate_sum = gu_sum[:, :, :unit].reshape(share, n_col * unit)
    up_sum = gu_sum[:, :, unit:].reshape(share, n_col * unit)
    sig = jax.nn.sigmoid(gate_sum)
    hidden_share = (gate_sum * sig * up_sum).astype(jnp.bfloat16)
    hidden = col_gather(hidden_share, n_col).reshape(count, n_col * unit)

    term = None
    for k, w in enumerate(down_rel):
        h = lax.dynamic_slice_in_dim(hidden, (me ^ k) * unit, unit, 1)
        t = jnp.dot(h, w, preferred_element_type=jnp.float32)
        term = t if term is None else term + t

    dh_part = place([contract_last(grad_full, w) for w in down_rel], me, 1)
    hidden_grad = col_reduce(dh_part, n_col).reshape(share, n_col * unit)
    grad_down = contract_first(hidden, grad_full).astype(jnp.bfloat16)

    gate_grad = (hidden_grad * up_sum * sig * (1.0 + gate_sum * (1.0 - sig))).astype(jnp.bfloat16)
    up_grad = (hidden_grad * gate_sum * sig).astype(jnp.bfloat16)
    joined_grad = jnp.concatenate(
        [gate_grad.reshape(share, n_col, unit), up_grad.reshape(share, n_col, unit)], axis=2
    )
    grads = col_gather(joined_grad, n_col).reshape(count, n_col, 2 * unit)

    in_part = None
    for k, w in enumerate(gu_rel):
        g = lax.dynamic_index_in_dim(grads, me ^ k, 1, keepdims=False)
        t = contract_last(g, w)
        in_part = t if in_part is None else in_part + t
    summed = reduce_rows(jnp.stack([term, in_part], axis=1), "row", n_row)
    output = summed[:, 0]
    input_grad = summed[:, 1]
    grad_gu = contract_first(full_tokens, grads.reshape(count, n_col * 2 * unit))
    grad_gu = grad_gu.reshape(-1, n_col, 2 * unit)
    grad_gate = grad_gu[:, :, :unit].reshape(-1, n_col * unit).astype(jnp.bfloat16)
    grad_up = grad_gu[:, :, unit:].reshape(-1, n_col * unit).astype(jnp.bfloat16)
    return (output, input_grad, grad_gate, grad_up, grad_down)


def solution(mesh):
    placed = (
        P("row", "col"),
        P(None, ("row", "col")),
        P(None, ("row", "col")),
        P(("row", "col"), None),
        P("row", "col"),
    )
    return jax.shard_map(
        shards,
        mesh=mesh,
        in_specs=placed,
        out_specs=(
            P("row", "col"),
            P("row", "col"),
            P("col", "row"),
            P("col", "row"),
            P("row", "col"),
        ),
        check_vma=False,
    )
```

```python
import jax
import jax.numpy as jnp
from jax import lax
from jax.sharding import PartitionSpec as P


def contract_last(left, right):
    return lax.dot_general(
        left, right, (((1,), (1,)), ((), ())), preferred_element_type=jnp.float32
    )


def contract_first(left, right):
    return lax.dot_general(
        left, right, (((0,), (0,)), ((), ())), preferred_element_type=jnp.float32
    )


def gather_rows(block, axis, n):
    spread = jnp.broadcast_to(block[None], (n,) + block.shape)
    got = lax.all_to_all(spread, axis, split_axis=0, concat_axis=0, tiled=True)
    return got.reshape((n * block.shape[0],) + block.shape[1:])


def reduce_rows(part, axis, n):
    pieces = part.reshape((n, part.shape[0] // n) + part.shape[1:]).astype(jnp.bfloat16)
    got = lax.all_to_all(pieces, axis, split_axis=0, concat_axis=0, tiled=True)
    return jnp.sum(got.astype(jnp.float32), axis=0)


def swap(x, k, n):
    return lax.ppermute(x, "col", perm=[(i, i ^ k) for i in range(n)])


def piece(x, index, size, axis):
    return lax.dynamic_slice_in_dim(x, index * size, size, axis)


def place(pieces, me, axis):
    shape = list(pieces[0].shape)
    shape.insert(axis, len(pieces))
    out = jnp.zeros(shape, pieces[0].dtype)
    for k, p in enumerate(pieces):
        start = [0] * len(shape)
        start[axis] = me ^ k
        out = lax.dynamic_update_slice(out, jnp.expand_dims(p, axis), start)
    return out


def col_scatter(x, axis, n):
    me = lax.axis_index("col")
    size = x.shape[axis] // n
    got = [piece(x, me, size, axis)]
    for k in range(1, n):
        got.append(swap(piece(x, me ^ k, size, axis), k, n))
    return got


def col_gather(x, n):
    me = lax.axis_index("col")
    got = [x] + [swap(x, k, n) for k in range(1, n)]
    return place(got, me, 0)


def col_reduce(x, n):
    me = lax.axis_index("col")
    size = x.shape[0] // n
    total = piece(x, me, size, 0)
    for k in range(1, n):
        total = total + swap(piece(x, me ^ k, size, 0), k, n)
    return total


def shards(tokens, gate_weight, up_weight, down_weight, out_grad):
    n_row = lax.axis_size("row")
    n_col = lax.axis_size("col")
    me = lax.axis_index("col")
    unit = gate_weight.shape[1]
    feat = gate_weight.shape[0] // n_col

    def gu_piece(index):
        return jnp.stack([piece(gate_weight, index, feat, 0), piece(up_weight, index, feat, 0)])

    gu_rel = [gu_piece(me)] + [swap(gu_piece(me ^ k), k, n_col) for k in range(1, n_col)]
    down_rel = col_scatter(down_weight, 1, n_col)

    both = gather_rows(jnp.stack([tokens, out_grad], axis=1), "row", n_row)
    full_tokens = both[:, 0]
    grad_full = both[:, 1]
    count = full_tokens.shape[0]

    gu_part = place(
        [
            jnp.concatenate(
                [jnp.dot(full_tokens, w[0], preferred_element_type=jnp.float32),
                 jnp.dot(full_tokens, w[1], preferred_element_type=jnp.float32)],
                axis=1,
            )
            for w in gu_rel
        ],
        me,
        1,
    )
    gu_sum = col_reduce(gu_part, n_col)
    share = gu_sum.shape[0]
    gate_sum = gu_sum[:, :, :unit].reshape(share, n_col * unit)
    up_sum = gu_sum[:, :, unit:].reshape(share, n_col * unit)
    sig = jax.nn.sigmoid(gate_sum)
    hidden_share = (gate_sum * sig * up_sum).astype(jnp.bfloat16)
    hidden = col_gather(hidden_share, n_col).reshape(count, n_col * unit)

    term = None
    for k, w in enumerate(down_rel):
        h = lax.dynamic_slice_in_dim(hidden, (me ^ k) * unit, unit, 1)
        t = jnp.dot(h, w, preferred_element_type=jnp.float32)
        term = t if term is None else term + t

    dh_part = place([contract_last(grad_full, w) for w in down_rel], me, 1)
    hidden_grad = col_reduce(dh_part, n_col).reshape(share, n_col * unit)
    grad_down = contract_first(hidden, grad_full).astype(jnp.bfloat16)

    gate_grad = (hidden_grad * up_sum * sig * (1.0 + gate_sum * (1.0 - sig))).astype(jnp.bfloat16)
    up_grad = (hidden_grad * gate_sum * sig).astype(jnp.bfloat16)
    joined_grad = jnp.concatenate(
        [gate_grad.reshape(share, n_col, unit), up_grad.reshape(share, n_col, unit)], axis=2
    )
    grads = col_gather(joined_grad, n_col).reshape(count, n_col, 2 * unit)

    in_part = None
    for k, w in enumerate(gu_rel):
        g = lax.dynamic_index_in_dim(grads, me ^ k, 1, keepdims=False)
        t = contract_last(g[:, :unit], w[0]) + contract_last(g[:, unit:], w[1])
        in_part = t if in_part is None else in_part + t
    summed = reduce_rows(jnp.stack([term, in_part], axis=1), "row", n_row)
    output = summed[:, 0]
    input_grad = summed[:, 1]
    grad_gu = contract_first(full_tokens, grads.reshape(count, n_col * 2 * unit))
    grad_gu = grad_gu.reshape(-1, n_col, 2 * unit)
    grad_gate = grad_gu[:, :, :unit].reshape(-1, n_col * unit).astype(jnp.bfloat16)
    grad_up = grad_gu[:, :, unit:].reshape(-1, n_col * unit).astype(jnp.bfloat16)
    return (output, input_grad, grad_gate, grad_up, grad_down)


def solution(mesh):
    placed = (
        P("row", "col"),
        P(None, ("row", "col")),
        P(None, ("row", "col")),
        P(("row", "col"), None),
        P("row", "col"),
    )
    return jax.shard_map(
        shards,
        mesh=mesh,
        in_specs=placed,
        out_specs=(
            P("row", "col"),
            P("row", "col"),
            P("col", "row"),
            P("col", "row"),
            P("row", "col"),
        ),
        check_vma=False,
    )
```

```python
import jax
import jax.numpy as jnp
from jax import lax
from jax.sharding import PartitionSpec as P


def contract_last(left, right):
    return lax.dot_general(
        left, right, (((1,), (1,)), ((), ())), preferred_element_type=jnp.float32
    )


def contract_first(left, right):
    return lax.dot_general(
        left, right, (((0,), (0,)), ((), ())), preferred_element_type=jnp.float32
    )


def gather_rows(block, axis, n):
    spread = jnp.broadcast_to(block[None], (n,) + block.shape)
    got = lax.all_to_all(spread, axis, split_axis=0, concat_axis=0, tiled=True)
    return got.reshape((n * block.shape[0],) + block.shape[1:])


def reduce_rows(part, axis, n):
    pieces = part.reshape((n, part.shape[0] // n) + part.shape[1:]).astype(jnp.bfloat16)
    got = lax.all_to_all(pieces, axis, split_axis=0, concat_axis=0, tiled=True)
    return jnp.sum(got.astype(jnp.float32), axis=0)


def swap(x, k, n):
    return lax.ppermute(x, "col", perm=[(i, i ^ k) for i in range(n)])


def piece(x, index, size, axis):
    return lax.dynamic_slice_in_dim(x, index * size, size, axis)


def place(pieces, me, axis):
    shape = list(pieces[0].shape)
    shape.insert(axis, len(pieces))
    out = jnp.zeros(shape, pieces[0].dtype)
    for k, p in enumerate(pieces):
        start = [0] * len(shape)
        start[axis] = me ^ k
        out = lax.dynamic_update_slice(out, jnp.expand_dims(p, axis), start)
    return out


def col_scatter(x, axis, n):
    me = lax.axis_index("col")
    size = x.shape[axis] // n
    got = [piece(x, me, size, axis)]
    for k in range(1, n):
        got.append(swap(piece(x, me ^ k, size, axis), k, n))
    return got


def col_gather(x, n):
    me = lax.axis_index("col")
    got = [x] + [swap(x, k, n) for k in range(1, n)]
    return place(got, me, 0)


def col_reduce(x, n):
    me = lax.axis_index("col")
    size = x.shape[0] // n
    total = piece(x, me, size, 0)
    for k in range(1, n):
        total = total + swap(piece(x, me ^ k, size, 0), k, n)
    return total


def shards(tokens, gate_weight, up_weight, down_weight, out_grad):
    n_row = lax.axis_size("row")
    n_col = lax.axis_size("col")
    me = lax.axis_index("col")
    unit = gate_weight.shape[1]
    feat = gate_weight.shape[0] // n_col

    def gu_piece(index):
        return jnp.stack([piece(gate_weight, index, feat, 0), piece(up_weight, index, feat, 0)])

    down_rel = col_scatter(down_weight, 1, n_col)
    gu_out = [gu_piece(me ^ k) for k in range(n_col)]
    gu_out, down_rel = lax.optimization_barrier((gu_out, down_rel))
    gu_rel = [gu_out[0]] + [swap(gu_out[k], k, n_col) for k in range(1, n_col)]

    both = gather_rows(jnp.stack([tokens, out_grad], axis=1), "row", n_row)
    full_tokens = both[:, 0]
    grad_full = both[:, 1]
    count = full_tokens.shape[0]

    gu_part = place(
        [
            jnp.concatenate(
                [jnp.dot(full_tokens, w[0], preferred_element_type=jnp.float32),
                 jnp.dot(full_tokens, w[1], preferred_element_type=jnp.float32)],
                axis=1,
            )
            for w in gu_rel
        ],
        me,
        1,
    )
    gu_sum = col_reduce(gu_part, n_col)
    share = gu_sum.shape[0]
    gate_sum = gu_sum[:, :, :unit].reshape(share, n_col * unit)
    up_sum = gu_sum[:, :, unit:].reshape(share, n_col * unit)
    sig = jax.nn.sigmoid(gate_sum)
    hidden_share = (gate_sum * sig * up_sum).astype(jnp.bfloat16)
    hidden = col_gather(hidden_share, n_col).reshape(count, n_col * unit)

    term = None
    for k, w in enumerate(down_rel):
        h = lax.dynamic_slice_in_dim(hidden, (me ^ k) * unit, unit, 1)
        t = jnp.dot(h, w, preferred_element_type=jnp.float32)
        term = t if term is None else term + t

    dh_part = place([contract_last(grad_full, w) for w in down_rel], me, 1)
    hidden_grad = col_reduce(dh_part, n_col).reshape(share, n_col * unit)
    grad_down = contract_first(hidden, grad_full).astype(jnp.bfloat16)

    gate_grad = (hidden_grad * up_sum * sig * (1.0 + gate_sum * (1.0 - sig))).astype(jnp.bfloat16)
    up_grad = (hidden_grad * gate_sum * sig).astype(jnp.bfloat16)
    joined_grad = jnp.concatenate(
        [gate_grad.reshape(share, n_col, unit), up_grad.reshape(share, n_col, unit)], axis=2
    )
    grads = col_gather(joined_grad, n_col).reshape(count, n_col, 2 * unit)

    in_part = None
    for k, w in enumerate(gu_rel):
        g = lax.dynamic_index_in_dim(grads, me ^ k, 1, keepdims=False)
        t = contract_last(g[:, :unit], w[0]) + contract_last(g[:, unit:], w[1])
        in_part = t if in_part is None else in_part + t
    summed = reduce_rows(jnp.stack([term, in_part], axis=1), "row", n_row)
    output = summed[:, 0]
    input_grad = summed[:, 1]
    grad_gu = contract_first(full_tokens, grads.reshape(count, n_col * 2 * unit))
    grad_gu = grad_gu.reshape(-1, n_col, 2 * unit)
    grad_gate = grad_gu[:, :, :unit].reshape(-1, n_col * unit).astype(jnp.bfloat16)
    grad_up = grad_gu[:, :, unit:].reshape(-1, n_col * unit).astype(jnp.bfloat16)
    return (output, input_grad, grad_gate, grad_up, grad_down)


def solution(mesh):
    placed = (
        P("row", "col"),
        P(None, ("row", "col")),
        P(None, ("row", "col")),
        P(("row", "col"), None),
        P("row", "col"),
    )
    return jax.shard_map(
        shards,
        mesh=mesh,
        in_specs=placed,
        out_specs=(
            P("row", "col"),
            P("row", "col"),
            P("col", "row"),
            P("col", "row"),
            P("row", "col"),
        ),
        check_vma=False,
    )
```

```python
import jax
import jax.numpy as jnp
from jax import lax
from jax.sharding import PartitionSpec as P


def contract_last(left, right):
    return lax.dot_general(
        left, right, (((1,), (1,)), ((), ())), preferred_element_type=jnp.float32
    )


def contract_first(left, right):
    return lax.dot_general(
        left, right, (((0,), (0,)), ((), ())), preferred_element_type=jnp.float32
    )


def gather_rows(block, axis, n):
    spread = jnp.broadcast_to(block[None], (n,) + block.shape)
    got = lax.all_to_all(spread, axis, split_axis=0, concat_axis=0, tiled=True)
    return got.reshape((n * block.shape[0],) + block.shape[1:])


def reduce_rows(part, axis, n):
    pieces = part.reshape((n, part.shape[0] // n) + part.shape[1:]).astype(jnp.bfloat16)
    got = lax.all_to_all(pieces, axis, split_axis=0, concat_axis=0, tiled=True)
    return jnp.sum(got.astype(jnp.float32), axis=0)


def swap(x, k, n):
    return lax.ppermute(x, "col", perm=[(i, i ^ k) for i in range(n)])


def piece(x, index, size, axis):
    return lax.dynamic_slice_in_dim(x, index * size, size, axis)


def place(pieces, me, axis):
    shape = list(pieces[0].shape)
    shape.insert(axis, len(pieces))
    out = jnp.zeros(shape, pieces[0].dtype)
    for k, p in enumerate(pieces):
        start = [0] * len(shape)
        start[axis] = me ^ k
        out = lax.dynamic_update_slice(out, jnp.expand_dims(p, axis), start)
    return out


def col_scatter(x, axis, n):
    me = lax.axis_index("col")
    size = x.shape[axis] // n
    got = [piece(x, me, size, axis)]
    for k in range(1, n):
        got.append(swap(piece(x, me ^ k, size, axis), k, n))
    return got


def col_gather(x, n):
    me = lax.axis_index("col")
    got = [x] + [swap(x, k, n) for k in range(1, n)]
    return place(got, me, 0)


def col_reduce(x, n):
    me = lax.axis_index("col")
    size = x.shape[0] // n
    total = piece(x, me, size, 0)
    for k in range(1, n):
        total = total + swap(piece(x, me ^ k, size, 0), k, n)
    return total


def shards(tokens, gate_weight, up_weight, down_weight, out_grad):
    n_row = lax.axis_size("row")
    n_col = lax.axis_size("col")
    me = lax.axis_index("col")
    unit = gate_weight.shape[1]
    feat = gate_weight.shape[0] // n_col

    def gu_piece(index):
        return jnp.stack([piece(gate_weight, index, feat, 0), piece(up_weight, index, feat, 0)])

    gu_rel = [gu_piece(me)] + [swap(gu_piece(me ^ k), k, n_col) for k in range(1, n_col)]
    down_out = [piece(down_weight, me ^ k, feat, 1) for k in range(n_col)]
    down_out, first = lax.optimization_barrier((down_out, gu_rel[2]))
    gu_rel[2] = first
    down_rel = [down_out[0]] + [swap(down_out[k], k, n_col) for k in range(1, n_col)]

    both = gather_rows(jnp.stack([tokens, out_grad], axis=1), "row", n_row)
    full_tokens = both[:, 0]
    grad_full = both[:, 1]
    count = full_tokens.shape[0]

    gu_part = place(
        [
            jnp.concatenate(
                [jnp.dot(full_tokens, w[0], preferred_element_type=jnp.float32),
                 jnp.dot(full_tokens, w[1], preferred_element_type=jnp.float32)],
                axis=1,
            )
            for w in gu_rel
        ],
        me,
        1,
    )
    gu_sum = col_reduce(gu_part, n_col)
    share = gu_sum.shape[0]
    gate_sum = gu_sum[:, :, :unit].reshape(share, n_col * unit)
    up_sum = gu_sum[:, :, unit:].reshape(share, n_col * unit)
    sig = jax.nn.sigmoid(gate_sum)
    hidden_share = (gate_sum * sig * up_sum).astype(jnp.bfloat16)
    hidden = col_gather(hidden_share, n_col).reshape(count, n_col * unit)

    term = None
    for k, w in enumerate(down_rel):
        h = lax.dynamic_slice_in_dim(hidden, (me ^ k) * unit, unit, 1)
        t = jnp.dot(h, w, preferred_element_type=jnp.float32)
        term = t if term is None else term + t

    dh_part = place([contract_last(grad_full, w) for w in down_rel], me, 1)
    hidden_grad = col_reduce(dh_part, n_col).reshape(share, n_col * unit)
    grad_down = contract_first(hidden, grad_full).astype(jnp.bfloat16)

    gate_grad = (hidden_grad * up_sum * sig * (1.0 + gate_sum * (1.0 - sig))).astype(jnp.bfloat16)
    up_grad = (hidden_grad * gate_sum * sig).astype(jnp.bfloat16)
    joined_grad = jnp.concatenate(
        [gate_grad.reshape(share, n_col, unit), up_grad.reshape(share, n_col, unit)], axis=2
    )
    grads = col_gather(joined_grad, n_col).reshape(count, n_col, 2 * unit)

    in_part = None
    for k, w in enumerate(gu_rel):
        g = lax.dynamic_index_in_dim(grads, me ^ k, 1, keepdims=False)
        t = contract_last(g[:, :unit], w[0]) + contract_last(g[:, unit:], w[1])
        in_part = t if in_part is None else in_part + t
    summed = reduce_rows(jnp.stack([term, in_part], axis=1), "row", n_row)
    output = summed[:, 0]
    input_grad = summed[:, 1]
    grad_gu = contract_first(full_tokens, grads.reshape(count, n_col * 2 * unit))
    grad_gu = grad_gu.reshape(-1, n_col, 2 * unit)
    grad_gate = grad_gu[:, :, :unit].reshape(-1, n_col * unit).astype(jnp.bfloat16)
    grad_up = grad_gu[:, :, unit:].reshape(-1, n_col * unit).astype(jnp.bfloat16)
    return (output, input_grad, grad_gate, grad_up, grad_down)


def solution(mesh):
    placed = (
        P("row", "col"),
        P(None, ("row", "col")),
        P(None, ("row", "col")),
        P(("row", "col"), None),
        P("row", "col"),
    )
    return jax.shard_map(
        shards,
        mesh=mesh,
        in_specs=placed,
        out_specs=(
            P("row", "col"),
            P("row", "col"),
            P("col", "row"),
            P("col", "row"),
            P("row", "col"),
        ),
        check_vma=False,
    )
```

```python
import jax
import jax.numpy as jnp
from jax import lax
from jax.sharding import PartitionSpec as P


def contract_last(left, right):
    return lax.dot_general(
        left, right, (((1,), (1,)), ((), ())), preferred_element_type=jnp.float32
    )


def contract_first(left, right):
    return lax.dot_general(
        left, right, (((0,), (0,)), ((), ())), preferred_element_type=jnp.float32
    )


def gather_rows(block, axis, n):
    spread = jnp.broadcast_to(block[None], (n,) + block.shape)
    got = lax.all_to_all(spread, axis, split_axis=0, concat_axis=0, tiled=True)
    return got.reshape((n * block.shape[0],) + block.shape[1:])


def reduce_rows(part, axis, n):
    pieces = part.reshape((n, part.shape[0] // n) + part.shape[1:]).astype(jnp.bfloat16)
    got = lax.all_to_all(pieces, axis, split_axis=0, concat_axis=0, tiled=True)
    return jnp.sum(got.astype(jnp.float32), axis=0)


def swap(x, k, n):
    return lax.ppermute(x, "col", perm=[(i, i ^ k) for i in range(n)])


def piece(x, index, size, axis):
    return lax.dynamic_slice_in_dim(x, index * size, size, axis)


def place(pieces, me, axis):
    shape = list(pieces[0].shape)
    shape.insert(axis, len(pieces))
    out = jnp.zeros(shape, pieces[0].dtype)
    for k, p in enumerate(pieces):
        start = [0] * len(shape)
        start[axis] = me ^ k
        out = lax.dynamic_update_slice(out, jnp.expand_dims(p, axis), start)
    return out


def col_scatter(x, axis, n):
    me = lax.axis_index("col")
    size = x.shape[axis] // n
    got = [piece(x, me, size, axis)]
    for k in range(1, n):
        got.append(swap(piece(x, me ^ k, size, axis), k, n))
    return got


def col_gather(x, n):
    me = lax.axis_index("col")
    got = [x] + [swap(x, k, n) for k in range(1, n)]
    return place(got, me, 0)


def col_reduce(x, n):
    me = lax.axis_index("col")
    size = x.shape[0] // n
    total = piece(x, me, size, 0)
    for k in range(1, n):
        total = total + swap(piece(x, me ^ k, size, 0), k, n)
    return total


def shards(tokens, gate_weight, up_weight, down_weight, out_grad):
    n_row = lax.axis_size("row")
    n_col = lax.axis_size("col")
    me = lax.axis_index("col")
    unit = gate_weight.shape[1]
    joined = jnp.concatenate([gate_weight, up_weight], axis=1)
    gu_rel = col_scatter(joined, 0, n_col)
    down_rel = col_scatter(down_weight, 1, n_col)

    both = gather_rows(jnp.stack([tokens, out_grad], axis=1), "row", n_row)
    full_tokens = both[:, 0]
    grad_full = both[:, 1]
    count = full_tokens.shape[0]

    gu_part = place([jnp.dot(full_tokens, w, preferred_element_type=jnp.float32) for w in gu_rel], me, 1)
    gu_sum = col_reduce(gu_part, n_col)
    share = gu_sum.shape[0]
    gate_sum = gu_sum[:, :, :unit].reshape(share, n_col * unit)
    up_sum = gu_sum[:, :, unit:].reshape(share, n_col * unit)
    sig = jax.nn.sigmoid(gate_sum)
    hidden_share = (gate_sum * sig * up_sum).astype(jnp.bfloat16)
    hidden = col_gather(hidden_share, n_col).reshape(count, n_col * unit)

    term = None
    for k, w in enumerate(down_rel):
        h = lax.dynamic_slice_in_dim(hidden, (me ^ k) * unit, unit, 1)
        t = jnp.dot(h, w, preferred_element_type=jnp.float32)
        term = t if term is None else term + t

    dh_part = place([contract_last(grad_full, w) for w in down_rel], me, 1)
    hidden_grad = col_reduce(dh_part, n_col).reshape(share, n_col * unit)
    grad_down = contract_first(hidden, grad_full).astype(jnp.bfloat16)

    gate_grad = (hidden_grad * up_sum * sig * (1.0 + gate_sum * (1.0 - sig))).astype(jnp.bfloat16)
    up_grad = (hidden_grad * gate_sum * sig).astype(jnp.bfloat16)
    joined_grad = jnp.concatenate(
        [gate_grad.reshape(share, n_col, unit), up_grad.reshape(share, n_col, unit)], axis=2
    )
    grads = col_gather(joined_grad, n_col).reshape(count, n_col, 2 * unit)

    gu_cat = jnp.concatenate(gu_rel, axis=1)
    g_rel = jnp.concatenate(
        [lax.dynamic_index_in_dim(grads, me ^ k, 1, keepdims=False) for k in range(n_col)], axis=1
    )
    in_part = contract_last(g_rel, gu_cat)
    summed = reduce_rows(jnp.stack([term, in_part], axis=1), "row", n_row)
    output = summed[:, 0]
    input_grad = summed[:, 1]
    grad_gu = contract_first(full_tokens, grads.reshape(count, n_col * 2 * unit))
    grad_gu = grad_gu.reshape(-1, n_col, 2 * unit)
    grad_gate = grad_gu[:, :, :unit].reshape(-1, n_col * unit).astype(jnp.bfloat16)
    grad_up = grad_gu[:, :, unit:].reshape(-1, n_col * unit).astype(jnp.bfloat16)
    return (output, input_grad, grad_gate, grad_up, grad_down)


def solution(mesh):
    placed = (
        P("row", "col"),
        P(None, ("row", "col")),
        P(None, ("row", "col")),
        P(("row", "col"), None),
        P("row", "col"),
    )
    return jax.shard_map(
        shards,
        mesh=mesh,
        in_specs=placed,
        out_specs=(
            P("row", "col"),
            P("row", "col"),
            P("col", "row"),
            P("col", "row"),
            P("row", "col"),
        ),
        check_vma=False,
    )
```

```python
import jax
import jax.numpy as jnp
from jax import lax
from jax.sharding import PartitionSpec as P


def contract_last(left, right):
    return lax.dot_general(
        left, right, (((1,), (1,)), ((), ())), preferred_element_type=jnp.float32
    )


def contract_first(left, right):
    return lax.dot_general(
        left, right, (((0,), (0,)), ((), ())), preferred_element_type=jnp.float32
    )


def gather_rows(block, axis, n):
    spread = jnp.broadcast_to(block[None], (n,) + block.shape)
    got = lax.all_to_all(spread, axis, split_axis=0, concat_axis=0, tiled=True)
    return got.reshape((n * block.shape[0],) + block.shape[1:])


def reduce_rows(part, axis, n):
    pieces = part.reshape((n, part.shape[0] // n) + part.shape[1:]).astype(jnp.bfloat16)
    got = lax.all_to_all(pieces, axis, split_axis=0, concat_axis=0, tiled=True)
    return jnp.sum(got.astype(jnp.float32), axis=0)


def swap(x, k, n):
    return lax.ppermute(x, "col", perm=[(i, i ^ k) for i in range(n)])


def piece(x, index, size, axis):
    return lax.dynamic_slice_in_dim(x, index * size, size, axis)


def place(pieces, me, axis):
    shape = list(pieces[0].shape)
    shape.insert(axis, len(pieces))
    out = jnp.zeros(shape, pieces[0].dtype)
    for k, p in enumerate(pieces):
        start = [0] * len(shape)
        start[axis] = me ^ k
        out = lax.dynamic_update_slice(out, jnp.expand_dims(p, axis), start)
    return out


def col_scatter(x, axis, n):
    me = lax.axis_index("col")
    size = x.shape[axis] // n
    got = [piece(x, me, size, axis)]
    for k in range(1, n):
        got.append(swap(piece(x, me ^ k, size, axis), k, n))
    return got


def col_gather(x, n):
    me = lax.axis_index("col")
    got = [x] + [swap(x, k, n) for k in range(1, n)]
    return place(got, me, 0)


def col_reduce(x, n):
    me = lax.axis_index("col")
    size = x.shape[0] // n
    total = piece(x, me, size, 0)
    for k in range(1, n):
        total = total + swap(piece(x, me ^ k, size, 0), k, n)
    return total


def shards(tokens, gate_weight, up_weight, down_weight, out_grad):
    n_row = lax.axis_size("row")
    n_col = lax.axis_size("col")
    me = lax.axis_index("col")
    unit = gate_weight.shape[1]
    joined = jnp.concatenate([gate_weight, up_weight], axis=1)
    gu_rel = col_scatter(joined, 0, n_col)
    down_rel = col_scatter(down_weight, 1, n_col)

    both = gather_rows(jnp.stack([tokens, out_grad], axis=1), "row", n_row)
    full_tokens = both[:, 0]
    grad_full = both[:, 1]
    count = full_tokens.shape[0]

    gu_part = place([jnp.dot(full_tokens, w, preferred_element_type=jnp.float32) for w in gu_rel], me, 1)
    gu_sum = col_reduce(gu_part, n_col)
    share = gu_sum.shape[0]
    gate_sum = gu_sum[:, :, :unit].reshape(share, n_col * unit)
    up_sum = gu_sum[:, :, unit:].reshape(share, n_col * unit)
    sig = jax.nn.sigmoid(gate_sum)
    hidden_share = (gate_sum * sig * up_sum).astype(jnp.bfloat16)


    dh_part = place([contract_last(grad_full, w) for w in down_rel], me, 1)
    hidden_grad = col_reduce(dh_part, n_col).reshape(share, n_col * unit)

    gate_grad = (hidden_grad * up_sum * sig * (1.0 + gate_sum * (1.0 - sig))).astype(jnp.bfloat16)
    up_grad = (hidden_grad * gate_sum * sig).astype(jnp.bfloat16)
    joined_grad = jnp.concatenate(
        [gate_grad.reshape(share, n_col, unit), up_grad.reshape(share, n_col, unit)], axis=2
    )
    both_col = col_gather(
        jnp.concatenate([hidden_share, joined_grad.reshape(share, n_col * 2 * unit)], axis=1), n_col
    ).reshape(count, n_col * 3 * unit)
    hidden = both_col[:, : n_col * unit]
    grads = both_col[:, n_col * unit :].reshape(count, n_col, 2 * unit)
    grad_down = contract_first(hidden, grad_full).astype(jnp.bfloat16)
    term = None
    for k, w in enumerate(down_rel):
        h = lax.dynamic_slice_in_dim(hidden, (me ^ k) * unit, unit, 1)
        t = jnp.dot(h, w, preferred_element_type=jnp.float32)
        term = t if term is None else term + t

    in_part = None
    for k, w in enumerate(gu_rel):
        g = lax.dynamic_index_in_dim(grads, me ^ k, 1, keepdims=False)
        t = contract_last(g, w)
        in_part = t if in_part is None else in_part + t
    summed = reduce_rows(jnp.stack([term, in_part], axis=1), "row", n_row)
    output = summed[:, 0]
    input_grad = summed[:, 1]
    grad_gu = contract_first(full_tokens, grads.reshape(count, n_col * 2 * unit))
    grad_gu = grad_gu.reshape(-1, n_col, 2 * unit)
    grad_gate = grad_gu[:, :, :unit].reshape(-1, n_col * unit).astype(jnp.bfloat16)
    grad_up = grad_gu[:, :, unit:].reshape(-1, n_col * unit).astype(jnp.bfloat16)
    return (output, input_grad, grad_gate, grad_up, grad_down)


def solution(mesh):
    placed = (
        P("row", "col"),
        P(None, ("row", "col")),
        P(None, ("row", "col")),
        P(("row", "col"), None),
        P("row", "col"),
    )
    return jax.shard_map(
        shards,
        mesh=mesh,
        in_specs=placed,
        out_specs=(
            P("row", "col"),
            P("row", "col"),
            P("col", "row"),
            P("col", "row"),
            P("row", "col"),
        ),
        check_vma=False,
    )
```

```python
import jax
import jax.numpy as jnp
from jax import lax
from jax.sharding import PartitionSpec as P


def contract_last(left, right):
    return lax.dot_general(
        left, right, (((1,), (1,)), ((), ())), preferred_element_type=jnp.float32
    )


def contract_first(left, right):
    return lax.dot_general(
        left, right, (((0,), (0,)), ((), ())), preferred_element_type=jnp.float32
    )


def gather_rows(block, axis, n):
    spread = jnp.broadcast_to(block[None], (n,) + block.shape)
    got = lax.all_to_all(spread, axis, split_axis=0, concat_axis=0, tiled=True)
    return got.reshape((n * block.shape[0],) + block.shape[1:])


def reduce_rows(part, axis, n):
    pieces = part.reshape((n, part.shape[0] // n) + part.shape[1:]).astype(jnp.bfloat16)
    got = lax.all_to_all(pieces, axis, split_axis=0, concat_axis=0, tiled=True)
    return jnp.sum(got.astype(jnp.float32), axis=0)


def swap(x, k, n):
    return lax.ppermute(x, "col", perm=[(i, i ^ k) for i in range(n)])


def piece(x, index, size, axis):
    return lax.dynamic_slice_in_dim(x, index * size, size, axis)


def place(pieces, me, axis):
    shape = list(pieces[0].shape)
    shape.insert(axis, len(pieces))
    out = jnp.zeros(shape, pieces[0].dtype)
    for k, p in enumerate(pieces):
        start = [0] * len(shape)
        start[axis] = me ^ k
        out = lax.dynamic_update_slice(out, jnp.expand_dims(p, axis), start)
    return out


def col_scatter(x, axis, n):
    me = lax.axis_index("col")
    size = x.shape[axis] // n
    got = [piece(x, me, size, axis)]
    for k in range(1, n):
        got.append(swap(piece(x, me ^ k, size, axis), k, n))
    return got


def col_gather(x, n):
    me = lax.axis_index("col")
    got = [x] + [swap(x, k, n) for k in range(1, n)]
    return place(got, me, 0)


def col_reduce(x, n):
    me = lax.axis_index("col")
    size = x.shape[0] // n
    total = piece(x, me, size, 0)
    for k in range(1, n):
        total = total + swap(piece(x, me ^ k, size, 0), k, n)
    return total


def shards(tokens, gate_weight, up_weight, down_weight, out_grad):
    n_row = lax.axis_size("row")
    n_col = lax.axis_size("col")
    me = lax.axis_index("col")
    unit = gate_weight.shape[1]
    joined = jnp.concatenate([gate_weight, up_weight], axis=1)
    gu_rel = col_scatter(joined, 0, n_col)
    down_rel = col_scatter(down_weight, 1, n_col)

    both = gather_rows(jnp.stack([tokens, out_grad], axis=1), "row", n_row)
    full_tokens = both[:, 0]
    grad_full = both[:, 1]
    count = full_tokens.shape[0]

    gu_part = place([jnp.dot(full_tokens, w, preferred_element_type=jnp.float32) for w in gu_rel], me, 1)
    gu_sum = col_reduce(gu_part, n_col)
    share = gu_sum.shape[0]
    gate_sum = gu_sum[:, :, :unit].reshape(share, n_col * unit)
    up_sum = gu_sum[:, :, unit:].reshape(share, n_col * unit)
    sig = jax.nn.sigmoid(gate_sum)
    hidden_share = (gate_sum * sig * up_sum).astype(jnp.bfloat16)
    hidden = col_gather(hidden_share, n_col).reshape(count, n_col * unit)

    term = None
    for k, w in enumerate(down_rel):
        h = lax.dynamic_slice_in_dim(hidden, (me ^ k) * unit, unit, 1)
        t = jnp.dot(h, w, preferred_element_type=jnp.float32)
        term = t if term is None else term + t

    dh_part = place([contract_last(grad_full, w) for w in down_rel], me, 1)
    hidden_grad = col_reduce(dh_part, n_col).reshape(share, n_col * unit)
    grad_down = contract_first(hidden, grad_full).astype(jnp.bfloat16)

    gate_grad = (hidden_grad * up_sum * sig * (1.0 + gate_sum * (1.0 - sig))).astype(jnp.bfloat16)
    up_grad = (hidden_grad * gate_sum * sig).astype(jnp.bfloat16)
    joined_grad = jnp.concatenate(
        [gate_grad.reshape(share, n_col, unit), up_grad.reshape(share, n_col, unit)], axis=2
    )
    arrived = [joined_grad] + [swap(joined_grad, k, n_col) for k in range(1, n_col)]
    grads = place(arrived, me, 0).reshape(count, n_col, 2 * unit)

    blocks = []
    for g_blk in arrived:
        acc = None
        for k, w in enumerate(gu_rel):
            g = lax.dynamic_index_in_dim(g_blk, me ^ k, 1, keepdims=False)
            t = contract_last(g, w)
            acc = t if acc is None else acc + t
        blocks.append(acc)
    in_part = place(blocks, me, 0).reshape(count, -1)
    summed = reduce_rows(jnp.stack([term, in_part], axis=1), "row", n_row)
    output = summed[:, 0]
    input_grad = summed[:, 1]
    grad_gu = contract_first(full_tokens, grads.reshape(count, n_col * 2 * unit))
    grad_gu = grad_gu.reshape(-1, n_col, 2 * unit)
    grad_gate = grad_gu[:, :, :unit].reshape(-1, n_col * unit).astype(jnp.bfloat16)
    grad_up = grad_gu[:, :, unit:].reshape(-1, n_col * unit).astype(jnp.bfloat16)
    return (output, input_grad, grad_gate, grad_up, grad_down)


def solution(mesh):
    placed = (
        P("row", "col"),
        P(None, ("row", "col")),
        P(None, ("row", "col")),
        P(("row", "col"), None),
        P("row", "col"),
    )
    return jax.shard_map(
        shards,
        mesh=mesh,
        in_specs=placed,
        out_specs=(
            P("row", "col"),
            P("row", "col"),
            P("col", "row"),
            P("col", "row"),
            P("row", "col"),
        ),
        check_vma=False,
    )
```
